256 devices in a mesh: layer: 32 (over z, x), row: 2 (over core), col: 4 (over y).
Axes of the slice: x: 4, y: 4, z: 8, core: 2. Of those that a mesh axis runs over, the one named last changes fastest.
Arguments:
- left_factor: float32 [2048, 65536], P('row', ('layer', 'col')), may hold values from -6 to 6
- right_factor: float32 [65536, 4096], P(('layer', 'row'), 'col'), may hold values from -0.15625 to 0.15625
- left_pattern: int32 [32, 1024], P('row', ('layer', 'col')), may hold values 0 or 1
- right_pattern: int32 [1024, 64], P(('layer', 'row'), 'col'), may hold values 0 or 1
- product_pattern: int32 [32, 64], P('row', 'col'), may hold values 0 or 1
Outputs:
- product: float32 [2048, 4096], P(('layer', 'row'), 'col')
The draws below stay inside these ranges and needn't reach their ends.
All inputs are finite; a program needn't handle non-finite values. No bound on the sum of `left_pattern` or of `right_pattern` or of `product_pattern` on one device may be relied on, other than what follows from the above.
Results may differ from the reference program's by a relative error of at most 0.000092.
Values sent between devices are 32-bit elements; how exact they have to be, the bound alone decides.
No kernel may reach another device: no remote copies, remote signals or barrier semaphores. Data moves between devices by JAX's collectives and lax.ppermute only.
A program may use at most 128 MiB of HBM per device.

```python
import jax
import jax.numpy as jnp
from jax import lax

BS = 64
RB = 16
M = 2048
N = 4096
K = 65536
MBL = 32
NBL = 64
KBL = 1024
N_LAYER = 32
N_ROW = 2


def touch_ends(drawn, own_key, smallest, top_value):
    shape = drawn.shape
    spot = [jax.random.randint(jax.random.fold_in(own_key, axis), (), 0, shape[axis]) for axis in range(len(shape))]
    drawn = drawn.at[tuple(spot)].set(smallest)
    longest = shape.index(max(shape))
    spot[longest] = (spot[longest] + 1) % shape[longest]
    return drawn.at[tuple(spot)].set(top_value)


def shard_levels(key, shape, split, smallest, top_value):
    def one(axis_at, blocks):
        heights = jax.random.uniform(jax.random.fold_in(jax.random.fold_in(key, 6), axis_at), (blocks,), jnp.float32, smallest / len(split), top_value / len(split))
        return jnp.repeat(jnp.exp(heights), shape[axis_at] // blocks).reshape((-1,) + (1,) * (len(shape) - axis_at - 1))

    level = one(*split[0])
    for cut in split[1:]:
        level = level * one(*cut)
    return level


def gaussian(stream_key, extent, deviation, most, pieces=(), dtype=jnp.bfloat16):
    entries = jax.random.normal(stream_key, extent, jnp.float32) * deviation
    if len(pieces) > 0:
        entries = shard_levels(stream_key, extent, pieces, -0.22, 0.18) * entries
    return jnp.clip(entries, min=-most, max=most).astype(dtype)


def setup_inputs(seed: int = 0) -> dict:
    key_list = jax.random.split(jax.random.key(seed), 6)
    left_factor = gaussian(key_list[0], (M, K), 1.0, 6.0, ((0, 2), (1, 128)), jnp.float32)
    right_factor = gaussian(key_list[1], (K, N), (K // 45) ** -0.5, 0.15625, ((0, 64), (1, 4)), jnp.float32)
    left_pattern = touch_ends((jax.random.randint(key_list[2], (MBL, KBL), 0, 20) < 3).astype(jnp.int32), jax.random.fold_in(key_list[2], 1), 0, 1)
    right_pattern = touch_ends((jax.random.randint(key_list[3], (KBL, NBL), 0, 20) < 3).astype(jnp.int32), jax.random.fold_in(key_list[3], 1), 0, 1)
    product_pattern = touch_ends((jax.random.randint(key_list[4], (MBL, NBL), 0, 3) < 1).astype(jnp.int32), jax.random.fold_in(key_list[4], 1), 0, 1)
    return dict(left_factor=left_factor, right_factor=right_factor, left_pattern=left_pattern, right_pattern=right_pattern, product_pattern=product_pattern)


def expand(pattern):
    return jnp.repeat(jnp.repeat(pattern.astype(jnp.float32), BS, axis=0), BS, axis=1)


def reference(left_factor, right_factor, left_pattern, right_pattern, product_pattern):
    left = left_factor * expand(left_pattern)
    right = right_factor * expand(right_pattern)
    full = jnp.dot(left, right, preferred_element_type=jnp.float32, precision=lax.Precision.HIGHEST)
    filtered = full * expand(product_pattern)
    slab = RB * BS // N_LAYER
    return filtered.reshape(N_ROW, N_LAYER, slab, N).transpose(1, 0, 2, 3).reshape(M, N)
```

```python
import jax
import jax.numpy as jnp
from jax import lax
from jax.sharding import Mesh
from jax.sharding import PartitionSpec as P

BS = 64


def expand(pattern):
    return jnp.repeat(jnp.repeat(pattern.astype(jnp.float32), BS, axis=0), BS, axis=1)


def body(left_factor, right_factor, left_pattern, right_pattern, product_pattern):
    left = left_factor * expand(left_pattern)
    right = right_factor * expand(right_pattern)
    left_whole = lax.all_gather(left, "col", axis=1, tiled=True)
    partial_sum = jnp.dot(
        left_whole,
        lax.all_gather(right, "row", axis=0, tiled=True),
        preferred_element_type=jnp.float32,
        precision=lax.Precision.HIGHEST,
    )
    kept = partial_sum * expand(product_pattern)
    kept = lax.psum_scatter(kept, "lz", scatter_dimension=0, tiled=True)
    return lax.psum_scatter(kept, "lx", scatter_dimension=0, tiled=True)


def solution(mesh):
    n_layer, n_row, n_col = mesh.devices.shape
    n_x = 4 if n_layer % 4 == 0 else 1
    split = Mesh(mesh.devices.reshape(n_layer // n_x, n_x, n_row, n_col), ("lz", "lx", "row", "col"))
    layer = ("lz", "lx")
    return jax.shard_map(
        body,
        mesh=split,
        in_specs=(
            P("row", (*layer, "col")),
            P((*layer, "row"), "col"),
            P("row", (*layer, "col")),
            P((*layer, "row"), "col"),
            P("row", "col"),
        ),
        out_specs=P((*layer, "row"), "col"),
        check_vma=False,
    )
```

```python
import jax
import jax.numpy as jnp
from jax import lax
from jax.sharding import Mesh
from jax.sharding import PartitionSpec as P

BS = 64
CHUNKS = 1
PRECISION = lax.Precision.HIGH
PERMUTE_GATHER = True
PERMUTE_RIGHT = False


def expand(pattern):
    return jnp.repeat(jnp.repeat(pattern.astype(jnp.float32), BS, axis=0), BS, axis=1)


def body(left_factor, right_factor, left_pattern, right_pattern, product_pattern):
    n_col = lax.axis_size("col")
    col = lax.axis_index("col")
    n_layer = lax.axis_size("lz") * lax.axis_size("lx")
    rows, k_piece = left_factor.shape
    slab = rows // n_layer
    left = left_factor * expand(left_pattern)
    right = right_factor * expand(right_pattern)
    if PERMUTE_RIGHT:
        n_row = lax.axis_size("row")
        other = lax.ppermute(right, "row", [(j, (j + 1) % n_row) for j in range(n_row)])
        row = lax.axis_index("row")
        right_whole = jnp.where(row == 0, jnp.concatenate([right, other]), jnp.concatenate([other, right]))
    else:
        right_whole = lax.all_gather(right, "row", axis=0, tiled=True)
    if PERMUTE_GATHER:
        right_by_shift = [
            lax.dynamic_slice_in_dim(right_whole, ((col - s) % n_col) * k_piece, k_piece, axis=0)
            for s in range(n_col)
        ]
    step = slab // CHUNKS
    by_layer = left.reshape(n_layer, slab, k_piece)
    outs = []
    for h in range(CHUNKS):
        part = by_layer[:, h * step:(h + 1) * step].reshape(n_layer * step, k_piece)
        if PERMUTE_GATHER:
            acc = jnp.dot(part, right_by_shift[0], preferred_element_type=jnp.float32, precision=PRECISION)
            for s in range(1, n_col):
                got = lax.ppermute(part, "col", [(j, (j + s) % n_col) for j in range(n_col)])
                acc = acc + jnp.dot(got, right_by_shift[s], preferred_element_type=jnp.float32, precision=PRECISION)
        else:
            whole = lax.all_gather(part, "col", axis=1, tiled=True)
            acc = jnp.dot(whole, right_whole, preferred_element_type=jnp.float32, precision=PRECISION)
        acc = lax.psum_scatter(acc, "lz", scatter_dimension=0, tiled=True)
        outs.append(lax.psum_scatter(acc, "lx", scatter_dimension=0, tiled=True))
    summed = jnp.concatenate(outs, axis=0) if CHUNKS > 1 else outs[0]
    layer = lax.axis_index("lz") * lax.axis_size("lx") + lax.axis_index("lx")
    keep = lax.dynamic_index_in_dim(product_pattern, (layer * slab) // BS, axis=0, keepdims=True)
    keep = jnp.repeat(keep.astype(jnp.float32), BS, axis=1)
    return summed * keep


def solution(mesh):
    n_layer, n_row, n_col = mesh.devices.shape
    n_x = 4 if n_layer % 4 == 0 else 1
    split = Mesh(mesh.devices.reshape(n_layer // n_x, n_x, n_row, n_col), ("lz", "lx", "row", "col"))
    layer = ("lz", "lx")
    return jax.shard_map(
        body,
        mesh=split,
        in_specs=(
            P("row", (*layer, "col")),
            P((*layer, "row"), "col"),
            P("row", (*layer, "col")),
            P((*layer, "row"), "col"),
            P("row", "col"),
        ),
        out_specs=P((*layer, "row"), "col"),
        check_vma=False,
    )
```

```python
import jax
import jax.numpy as jnp
from jax import lax
from jax.sharding import Mesh
from jax.sharding import PartitionSpec as P

BS = 64
CHUNKS = 1
PRECISION = lax.Precision.HIGH
PERMUTE_GATHER = True
PERMUTE_RIGHT = False


def expand(pattern):
    return jnp.repeat(jnp.repeat(pattern.astype(jnp.float32), BS, axis=0), BS, axis=1)


def body(left_factor, right_factor, left_pattern, right_pattern, product_pattern):
    n_col = lax.axis_size("col")
    col = lax.axis_index("col")
    n_layer = lax.axis_size("lz") * lax.axis_size("lx")
    rows, k_piece = left_factor.shape
    slab = rows // n_layer
    left = left_factor * expand(left_pattern)
    right = right_factor * expand(right_pattern)
    if PERMUTE_RIGHT:
        n_row = lax.axis_size("row")
        other = lax.ppermute(right, "row", [(j, (j + 1) % n_row) for j in range(n_row)])
        row = lax.axis_index("row")
        right_whole = jnp.where(row == 0, jnp.concatenate([right, other]), jnp.concatenate([other, right]))
    else:
        right_whole = lax.all_gather(right, "row", axis=0, tiled=True)
    if PERMUTE_GATHER:
        right_by_shift = [
            lax.dynamic_slice_in_dim(right_whole, ((col - s) % n_col) * k_piece, k_piece, axis=0)
            for s in range(n_col)
        ]
    step = slab // CHUNKS
    by_layer = left.reshape(n_layer, slab, k_piece)
    outs = []
    for h in range(CHUNKS):
        part = by_layer[:, h * step:(h + 1) * step].reshape(n_layer * step, k_piece)
        if PERMUTE_GATHER:
            acc = jnp.dot(part, right_by_shift[0], preferred_element_type=jnp.float32, precision=PRECISION)
            up = [(j, (j + 1) % n_col) for j in range(n_col)]
            down = [(j, (j - 1) % n_col) for j in range(n_col)]
            from_below = lax.ppermute(part, "col", up)
            from_above = lax.ppermute(part, "col", down)
            acc = acc + jnp.dot(from_below, right_by_shift[1], preferred_element_type=jnp.float32, precision=PRECISION)
            acc = acc + jnp.dot(from_above, right_by_shift[n_col - 1], preferred_element_type=jnp.float32, precision=PRECISION)
            half = k_piece // 2
            far = right_by_shift[2]
            first = lax.ppermute(from_below[:, :half], "col", up)
            second = lax.ppermute(from_above[:, half:], "col", down)
            acc = acc + jnp.dot(first, far[:half], preferred_element_type=jnp.float32, precision=PRECISION)
            acc = acc + jnp.dot(second, far[half:], preferred_element_type=jnp.float32, precision=PRECISION)
        else:
            whole = lax.all_gather(part, "col", axis=1, tiled=True)
            acc = jnp.dot(whole, right_whole, preferred_element_type=jnp.float32, precision=PRECISION)
        acc = lax.psum_scatter(acc, "lz", scatter_dimension=0, tiled=True)
        outs.append(lax.psum_scatter(acc, "lx", scatter_dimension=0, tiled=True))
    summed = jnp.concatenate(outs, axis=0) if CHUNKS > 1 else outs[0]
    layer = lax.axis_index("lz") * lax.axis_size("lx") + lax.axis_index("lx")
    keep = lax.dynamic_index_in_dim(product_pattern, (layer * slab) // BS, axis=0, keepdims=True)
    keep = jnp.repeat(keep.astype(jnp.float32), BS, axis=1)
    return summed * keep


def solution(mesh):
    n_layer, n_row, n_col = mesh.devices.shape
    n_x = 4 if n_layer % 4 == 0 else 1
    split = Mesh(mesh.devices.reshape(n_layer // n_x, n_x, n_row, n_col), ("lz", "lx", "row", "col"))
    layer = ("lz", "lx")
    return jax.shard_map(
        body,
        mesh=split,
        in_specs=(
            P("row", (*layer, "col")),
            P((*layer, "row"), "col"),
            P("row", (*layer, "col")),
            P((*layer, "row"), "col"),
            P("row", "col"),
        ),
        out_specs=P((*layer, "row"), "col"),
        check_vma=False,
    )
```

```python
import jax
import jax.numpy as jnp
from jax import lax
from jax.sharding import Mesh
from jax.sharding import PartitionSpec as P

BS = 64
CHUNKS = 1
PRECISION = lax.Precision.HIGH
PERMUTE_GATHER = True
PERMUTE_RIGHT = False


def expand(pattern):
    return jnp.repeat(jnp.repeat(pattern.astype(jnp.float32), BS, axis=0), BS, axis=1)


def body(left_factor, right_factor, left_pattern, right_pattern, product_pattern):
    n_col = lax.axis_size("col")
    col = lax.axis_index("col")
    n_layer = lax.axis_size("lz") * lax.axis_size("lx")
    rows, k_piece = left_factor.shape
    slab = rows // n_layer
    left = left_factor * expand(left_pattern)
    right = right_factor * expand(right_pattern)
    if PERMUTE_RIGHT:
        n_row = lax.axis_size("row")
        other = lax.ppermute(right, "row", [(j, (j + 1) % n_row) for j in range(n_row)])
        row = lax.axis_index("row")
        right_whole = jnp.where(row == 0, jnp.concatenate([right, other]), jnp.concatenate([other, right]))
    else:
        right_whole = lax.all_gather(right, "row", axis=0, tiled=True)
    if PERMUTE_GATHER:
        right_by_shift = [
            lax.dynamic_slice_in_dim(right_whole, ((col - s) % n_col) * k_piece, k_piece, axis=0)
            for s in range(n_col)
        ]
    step = slab // CHUNKS
    by_layer = left.reshape(n_layer, slab, k_piece)
    outs = []
    for h in range(CHUNKS):
        part = by_layer[:, h * step:(h + 1) * step].reshape(n_layer * step, k_piece)
        if PERMUTE_GATHER:
            acc = jnp.dot(part, right_by_shift[0], preferred_element_type=jnp.float32, precision=PRECISION)
            up = [(j, (j + 1) % n_col) for j in range(n_col)]
            down = [(j, (j - 1) % n_col) for j in range(n_col)]
            from_below = lax.ppermute(part, "col", up)
            from_above = lax.ppermute(part, "col", down)
            acc = acc + jnp.dot(from_below, right_by_shift[1], preferred_element_type=jnp.float32, precision=PRECISION)
            acc = acc + jnp.dot(from_above, right_by_shift[n_col - 1], preferred_element_type=jnp.float32, precision=PRECISION)
            half = k_piece // 2
            far = right_by_shift[2]
            first = lax.ppermute(from_below[:, :half], "col", up)
            second = lax.ppermute(from_above[:, half:], "col", down)
            acc = acc + jnp.dot(first, far[:half], preferred_element_type=jnp.float32, precision=PRECISION)
            acc = acc + jnp.dot(second, far[half:], preferred_element_type=jnp.float32, precision=PRECISION)
        else:
            whole = lax.all_gather(part, "col", axis=1, tiled=True)
            acc = jnp.dot(whole, right_whole, preferred_element_type=jnp.float32, precision=PRECISION)
        acc = lax.psum_scatter(acc, "lz", scatter_dimension=0, tiled=True)
        n_x = lax.axis_size("lx")
        blocks = lax.all_to_all(acc.reshape(n_x, acc.shape[0] // n_x, acc.shape[1]), "lx", 0, 0, tiled=True)
        outs.append(blocks.sum(axis=0))
    summed = jnp.concatenate(outs, axis=0) if CHUNKS > 1 else outs[0]
    layer = lax.axis_index("lz") * lax.axis_size("lx") + lax.axis_index("lx")
    keep = lax.dynamic_index_in_dim(product_pattern, (layer * slab) // BS, axis=0, keepdims=True)
    keep = jnp.repeat(keep.astype(jnp.float32), BS, axis=1)
    return summed * keep


def solution(mesh):
    n_layer, n_row, n_col = mesh.devices.shape
    n_x = 4 if n_layer % 4 == 0 else 1
    split = Mesh(mesh.devices.reshape(n_layer // n_x, n_x, n_row, n_col), ("lz", "lx", "row", "col"))
    layer = ("lz", "lx")
    return jax.shard_map(
        body,
        mesh=split,
        in_specs=(
            P("row", (*layer, "col")),
            P((*layer, "row"), "col"),
            P("row", (*layer, "col")),
            P((*layer, "row"), "col"),
            P("row", "col"),
        ),
        out_specs=P((*layer, "row"), "col"),
        check_vma=False,
    )
```

```python
import jax
import jax.numpy as jnp
from jax import lax
from jax.sharding import Mesh
from jax.sharding import PartitionSpec as P

BS = 64
CHUNKS = 1
PRECISION = lax.Precision.HIGH
PERMUTE_GATHER = True
PERMUTE_RIGHT = False


def expand(pattern):
    return jnp.repeat(jnp.repeat(pattern.astype(jnp.float32), BS, axis=0), BS, axis=1)


def body(left_factor, right_factor, left_pattern, right_pattern, product_pattern):
    n_col = lax.axis_size("col")
    col = lax.axis_index("col")
    n_layer = lax.axis_size("lz") * lax.axis_size("lx")
    rows, k_piece = left_factor.shape
    slab = rows // n_layer
    left = left_factor * expand(left_pattern)
    right = right_factor * expand(right_pattern)
    if PERMUTE_RIGHT:
        n_row = lax.axis_size("row")
        other = lax.ppermute(right, "row", [(j, (j + 1) % n_row) for j in range(n_row)])
        row = lax.axis_index("row")
        right_whole = jnp.where(row == 0, jnp.concatenate([right, other]), jnp.concatenate([other, right]))
    else:
        right_whole = lax.all_gather(right, "row", axis=0, tiled=True)
    if PERMUTE_GATHER:
        right_by_shift = [
            lax.dynamic_slice_in_dim(right_whole, ((col - s) % n_col) * k_piece, k_piece, axis=0)
            for s in range(n_col)
        ]
    step = slab // CHUNKS
    by_layer = left.reshape(n_layer, slab, k_piece)
    outs = []
    for h in range(CHUNKS):
        part = by_layer[:, h * step:(h + 1) * step].reshape(n_layer * step, k_piece)
        if PERMUTE_GATHER:
            acc = jnp.dot(part, right_by_shift[0], preferred_element_type=jnp.float32, precision=PRECISION)
            up = [(j, (j + 1) % n_col) for j in range(n_col)]
            down = [(j, (j - 1) % n_col) for j in range(n_col)]
            half = k_piece // 2
            below_a = lax.ppermute(part[:, :half], "col", up)
            above_b = lax.ppermute(part[:, half:], "col", down)
            below_b = lax.ppermute(part[:, half:], "col", up)
            above_a = lax.ppermute(part[:, :half], "col", down)
            near = right_by_shift[1]
            acc = acc + jnp.dot(below_a, near[:half], preferred_element_type=jnp.float32, precision=PRECISION)
            acc = acc + jnp.dot(below_b, near[half:], preferred_element_type=jnp.float32, precision=PRECISION)
            near = right_by_shift[n_col - 1]
            acc = acc + jnp.dot(above_a, near[:half], preferred_element_type=jnp.float32, precision=PRECISION)
            acc = acc + jnp.dot(above_b, near[half:], preferred_element_type=jnp.float32, precision=PRECISION)
            far = right_by_shift[2]
            first = lax.ppermute(below_a, "col", up)
            second = lax.ppermute(above_b, "col", down)
            acc = acc + jnp.dot(first, far[:half], preferred_element_type=jnp.float32, precision=PRECISION)
            acc = acc + jnp.dot(second, far[half:], preferred_element_type=jnp.float32, precision=PRECISION)
        else:
            whole = lax.all_gather(part, "col", axis=1, tiled=True)
            acc = jnp.dot(whole, right_whole, preferred_element_type=jnp.float32, precision=PRECISION)
        acc = lax.psum_scatter(acc, "lz", scatter_dimension=0, tiled=True)
        n_x = lax.axis_size("lx")
        blocks = lax.all_to_all(acc.reshape(n_x, acc.shape[0] // n_x, acc.shape[1]), "lx", 0, 0, tiled=True)
        outs.append(blocks.sum(axis=0))
    summed = jnp.concatenate(outs, axis=0) if CHUNKS > 1 else outs[0]
    layer = lax.axis_index("lz") * lax.axis_size("lx") + lax.axis_index("lx")
    keep = lax.dynamic_index_in_dim(product_pattern, (layer * slab) // BS, axis=0, keepdims=True)
    keep = jnp.repeat(keep.astype(jnp.float32), BS, axis=1)
    return summed * keep


def solution(mesh):
    n_layer, n_row, n_col = mesh.devices.shape
    n_x = 4 if n_layer % 4 == 0 else 1
    split = Mesh(mesh.devices.reshape(n_layer // n_x, n_x, n_row, n_col), ("lz", "lx", "row", "col"))
    layer = ("lz", "lx")
    return jax.shard_map(
        body,
        mesh=split,
        in_specs=(
            P("row", (*layer, "col")),
            P((*layer, "row"), "col"),
            P("row", (*layer, "col")),
            P((*layer, "row"), "col"),
            P("row", "col"),
        ),
        out_specs=P((*layer, "row"), "col"),
        check_vma=False,
    )
```
